256 devices in a mesh: ver: 16 (over y, x), row: 16 (over z, core).
Axes of the slice: x: 4, y: 4, z: 8, core: 2. Of those that a mesh axis runs over, the one named last changes fastest.
Arguments:
- embedding: bfloat16 [16, 32768, 512], P('ver', 'row'), may hold values from -48 to 48
- anchor_rows: int32 [16384], P('row'), may hold values from 0 to 32767, as said below
Outputs:
- aligned: bfloat16 [16, 32768, 512], P('ver', 'row')
The draws below stay inside these ranges and needn't reach their ends.
Inputs may be any that keep to these rules, and one draw needn't show every extreme that they name: `anchor_rows`: the k-th block of 1024 entries names rows k * 2048 to (k + 1) * 2048 - 1; rows may repeat.
All inputs are finite; a program needn't handle non-finite values.
Results may differ from the reference program's by a relative error of at most 0.0019.
The reference program's roundings to bfloat16 on the way count: a program that leaves them out, or rounds other values in their place, can miss the bound.
Values may be sent and summed in bfloat16 or wider, within the bound.
No kernel may reach another device: no remote copies, remote signals or barrier semaphores. Data moves between devices by JAX's collectives and lax.ppermute only.
A program may use at most 64 MiB of HBM per device.

```python
import math
import jax
import jax.numpy as jnp
from jax import lax

D = 512
TAB_DEV = 2048
ANC_DEV = 1024
ITERS = 12
VERSIONS = 16
ROWS = 32768
ANCHORS = 16384


def draw_anchor_rows(key, part):
    offsets = jax.random.randint(key, (ANCHORS,), 0, TAB_DEV, dtype=jnp.int32)
    position = jnp.arange(ANCHORS, dtype=jnp.int32) % ANC_DEV
    offsets = jnp.where(position == 0, 0, jnp.where(position == ANC_DEV - 1, TAB_DEV - 1, offsets))
    blocks = jnp.arange(ANCHORS, dtype=jnp.int32) // ANC_DEV
    return (blocks * TAB_DEV + offsets).astype(jnp.int32)


def fast_hadamard(values):
    column_count = values.shape[1]
    row_count = values.shape[0]
    stride = 1
    while stride < column_count:
        paired = values.reshape(row_count, column_count // (2 * stride), 2, stride)
        leading = paired[:, :, 0, :]
        second = paired[:, :, 1, :]
        values = jnp.stack([leading + second, leading - second], axis=2).reshape(row_count, column_count)
        stride = stride * 2
    return values * (1.0 / math.sqrt(column_count))


def random_signs(key):
    return (jax.random.randint(key, (1, D), 0, 2, dtype=jnp.int32) * 2 - 1).astype(jnp.float32)


def draw_embedding(key, part):
    base_key = jax.random.fold_in(key, 101)
    column_key = jax.random.fold_in(key, 202)
    row_index = jnp.arange(ROWS, dtype=jnp.int32)
    column_index = jnp.arange(D, dtype=jnp.int32)
    block_total = ROWS // TAB_DEV
    favoured = column_index[None, :] % block_total == row_index[:, None] // TAB_DEV
    boost = jnp.where(favoured, 2.0, 1.0).astype(jnp.float32)
    log_spread = 0.2
    base = jnp.clip(jax.random.normal(base_key, (ROWS, D), jnp.float32), -5.0, 5.0)
    column_scale = jnp.exp(jax.random.uniform(column_key, (1, D), jnp.float32, -log_spread, log_spread))
    base = base * column_scale * boost

    def one_version(version):
        version_key = jax.random.fold_in(key, 1000 + version)
        signs_first = random_signs(jax.random.fold_in(version_key, 1))
        signs_second = random_signs(jax.random.fold_in(version_key, 2))
        order = jax.random.permutation(jax.random.fold_in(version_key, 3), D)
        noise_key = jax.random.fold_in(version_key, 4)
        mixed = fast_hadamard(base * signs_first)
        mixed = jnp.take(mixed, order, axis=1)
        mixed = fast_hadamard(mixed * signs_second)
        noise = jnp.clip(jax.random.normal(noise_key, (ROWS, D), jnp.float32), -5.0, 5.0)
        return mixed + 0.06 * noise
    return lax.map(one_version, jnp.arange(VERSIONS, dtype=jnp.int32)).astype(jnp.bfloat16)


def setup_inputs(seed: int = 0) -> dict:
    arg_keys = jax.random.split(jax.random.key(seed), 3)
    embedding = draw_embedding(jax.random.fold_in(arg_keys[2], 71), 0)
    anchor_rows = draw_anchor_rows(jax.random.fold_in(arg_keys[2], 71), 0)
    return {"embedding": embedding, "anchor_rows": anchor_rows}


def polar_factor(cross_gram):
    frobenius = jnp.sqrt(jnp.sum(cross_gram * cross_gram) + 1e-06)
    iterate = cross_gram / frobenius
    for sweep_index in range(ITERS):
        square = jnp.dot(iterate.T, iterate, precision=lax.Precision.HIGHEST)
        iterate = 1.5 * iterate - 0.5 * jnp.dot(iterate, square, precision=lax.Precision.HIGHEST)
    return iterate

def reference(embedding, anchor_rows):
    slabs = embedding[:, anchor_rows, :]
    prefix = jnp.eye(D, dtype=jnp.float32)
    results = []
    for version in range(VERSIONS):
        if version > 0:
            cross_gram = jnp.dot(slabs[version].T, slabs[version - 1], preferred_element_type=jnp.float32)
            rotation = polar_factor(cross_gram)
            prefix = jnp.dot(rotation, prefix, precision=lax.Precision.HIGHEST)
        low = prefix.astype(jnp.bfloat16)
        results.append(jnp.dot(embedding[version], low, preferred_element_type=jnp.float32).astype(jnp.bfloat16))
    return jnp.stack(results, axis=0)
```

```python
import jax
import jax.numpy as jnp
from jax import lax
from jax.sharding import PartitionSpec as P

ITERS = 12
HIGHEST = lax.Precision.HIGHEST


def shifted(value, axis, steps):
    count = lax.axis_size(axis)
    return lax.ppermute(value, axis, [(source, source + steps) for source in range(count - steps)])


def swapped(value, axis, mask):
    count = lax.axis_size(axis)
    return lax.ppermute(value, axis, [(source, source ^ mask) for source in range(count)])


def summed_over(partial, axis):
    count = lax.axis_size(axis)
    pieces = partial.reshape(count, partial.shape[0] // count, partial.shape[1])
    reduced = lax.all_to_all(pieces, axis, 0, 0, tiled=False).sum(0)
    copies = jnp.broadcast_to(reduced[None], (count,) + reduced.shape)
    return lax.all_to_all(copies, axis, 0, 0, tiled=False).reshape(partial.shape)


def newton_update(sweep_index, iterate):
    square = jnp.dot(iterate.T, iterate, precision=HIGHEST)
    return 1.5 * iterate - 0.5 * jnp.dot(iterate, square, precision=HIGHEST)


def running_product(rotation, axis, core):
    count, mine = (lax.axis_size(axis), lax.axis_index(axis))
    half = rotation.shape[0] // 2
    product = rotation
    steps = 1
    while steps < count:
        sent = jnp.where(core == 0, product[:half], product[half:])
        received = shifted(sent, axis, steps)
        partner = swapped(received, "row", 1)
        earlier = jnp.where(
            core == 0,
            jnp.concatenate([received, partner]),
            jnp.concatenate([partner, received]),
        )
        longer = jnp.dot(product, earlier, precision=HIGHEST)
        product = jnp.where(mine >= steps, longer, product)
        steps *= 2
    return product


def per_device(embedding, anchor_rows):
    own_rows = embedding[0]
    width = own_rows.shape[1]
    positions = anchor_rows - lax.axis_index("row") * own_rows.shape[0]
    own_slab = jnp.take(own_rows, positions, axis=0)
    previous_slab = shifted(own_slab, "ver", 1)
    partial_gram = lax.dot_general(
        own_slab, previous_slab, (((0,), (0,)), ((), ())), preferred_element_type=jnp.float32
    )
    cross_gram = summed_over(partial_gram, "row")
    frobenius = jnp.sqrt(jnp.sum(cross_gram * cross_gram) + 1e-06)
    iterate = cross_gram / frobenius
    rotation = lax.fori_loop(0, ITERS, newton_update, iterate)
    identity_matrix = jnp.eye(width, dtype=jnp.float32)
    rotation = jnp.where(lax.axis_index("ver") == 0, identity_matrix, rotation)
    prefix = running_product(rotation, "ver", lax.axis_index("row") % 2)
    prefix_low = prefix.astype(jnp.bfloat16)
    aligned = jnp.dot(own_rows, prefix_low, preferred_element_type=jnp.float32).astype(jnp.bfloat16)
    return aligned[None]


def solution(mesh):
    return jax.shard_map(
        per_device,
        mesh=mesh,
        in_specs=(P("ver", "row", None), P("row")),
        out_specs=P("ver", "row", None),
        check_vma=False,
    )
```

```python
import jax
import jax.numpy as jnp
from jax import lax
from jax.sharding import Mesh, PartitionSpec as P

ITERS = 12
HIGHEST = lax.Precision.HIGHEST


def shifted(value, axis, steps):
    count = lax.axis_size(axis)
    return lax.ppermute(value, axis, [(source, source + steps) for source in range(count - steps)])


def swapped(value, axis, mask):
    count = lax.axis_size(axis)
    return lax.ppermute(value, axis, [(source, source ^ mask) for source in range(count)])


def halves(matrix, core):
    half = matrix.shape[0] // 2
    return jnp.where(core == 0, matrix[:half], matrix[half:]), jnp.where(core == 0, matrix[half:], matrix[:half])


def joined(mine, other, core):
    return jnp.where(core == 0, jnp.concatenate([mine, other]), jnp.concatenate([other, mine]))


def summed_over(partial, axis, core):
    mine, other = halves(partial, core)
    mine = mine + swapped(other, "core", 1)
    count = lax.axis_size(axis)
    pieces = mine.reshape(count, mine.shape[0] // count, mine.shape[1])
    reduced = lax.all_to_all(pieces, axis, 0, 0, tiled=False).sum(0)
    copies = jnp.broadcast_to(reduced[None], (count,) + reduced.shape)
    mine = lax.all_to_all(copies, axis, 0, 0, tiled=False).reshape(mine.shape)
    return joined(mine, swapped(mine, "core", 1), core)


def newton_update(sweep_index, iterate):
    square = jnp.dot(iterate.T, iterate, precision=HIGHEST)
    return 1.5 * iterate - 0.5 * jnp.dot(iterate, square, precision=HIGHEST)


def running_product(rotation, axis, core):
    count, mine = (lax.axis_size(axis), lax.axis_index(axis))
    product = rotation
    steps = 1
    while steps < count:
        received = shifted(halves(product, core)[0], axis, steps)
        earlier = joined(received, swapped(received, "core", 1), core)
        longer = jnp.dot(product, earlier, precision=HIGHEST)
        product = jnp.where(mine >= steps, longer, product)
        steps *= 2
    return product


def per_device(embedding, anchor_rows):
    own_rows = embedding[0]
    width = own_rows.shape[1]
    core = lax.axis_index("core")
    row_index = lax.axis_index("z") * lax.axis_size("core") + core
    positions = anchor_rows - row_index * own_rows.shape[0]
    own_slab = jnp.take(own_rows, positions, axis=0)
    previous_slab = shifted(own_slab, "ver", 1)
    partial_gram = lax.dot_general(
        own_slab, previous_slab, (((0,), (0,)), ((), ())), preferred_element_type=jnp.float32
    )
    cross_gram = summed_over(partial_gram, "z", core)
    frobenius = jnp.sqrt(jnp.sum(cross_gram * cross_gram) + 1e-06)
    iterate = cross_gram / frobenius
    rotation = lax.fori_loop(0, ITERS, newton_update, iterate)
    identity_matrix = jnp.eye(width, dtype=jnp.float32)
    rotation = jnp.where(lax.axis_index("ver") == 0, identity_matrix, rotation)
    prefix = running_product(rotation, "ver", core)
    prefix_low = prefix.astype(jnp.bfloat16)
    aligned = jnp.dot(own_rows, prefix_low, preferred_element_type=jnp.float32).astype(jnp.bfloat16)
    return aligned[None]


def solution(mesh):
    versions, rows = mesh.devices.shape
    cores = 2
    split_mesh = Mesh(mesh.devices.reshape(versions, rows // cores, cores), ("ver", "z", "core"))
    row = ("z", "core")
    return jax.shard_map(
        per_device,
        mesh=split_mesh,
        in_specs=(P("ver", row, None), P(row)),
        out_specs=P("ver", row, None),
        check_vma=False,
    )
```

```python
import jax
import jax.numpy as jnp
from jax import lax
from jax.sharding import Mesh, PartitionSpec as P

ITERS = 12
ROUGH_ITERS = 8
HIGHEST = lax.Precision.HIGHEST


def shifted(value, axis, steps):
    count = lax.axis_size(axis)
    return lax.ppermute(value, axis, [(source, source + steps) for source in range(count - steps)])


def swapped(value, axis, mask):
    count = lax.axis_size(axis)
    return lax.ppermute(value, axis, [(source, source ^ mask) for source in range(count)])


def halves(matrix, core):
    half = matrix.shape[0] // 2
    return jnp.where(core == 0, matrix[:half], matrix[half:]), jnp.where(core == 0, matrix[half:], matrix[:half])


def joined(mine, other, core):
    return jnp.where(core == 0, jnp.concatenate([mine, other]), jnp.concatenate([other, mine]))


def summed_over(partial, axis, core):
    mine, other = halves(partial, core)
    mine = mine + swapped(other, "core", 1)
    count = lax.axis_size(axis)
    pieces = mine.reshape(count, mine.shape[0] // count, mine.shape[1])
    reduced = lax.all_to_all(pieces, axis, 0, 0, tiled=False).sum(0)
    copies = jnp.broadcast_to(reduced[None], (count,) + reduced.shape)
    mine = lax.all_to_all(copies, axis, 0, 0, tiled=False).reshape(mine.shape)
    return joined(mine, swapped(mine, "core", 1), core)


def newton_update(precision):
    def update(sweep_index, iterate):
        square = jnp.dot(iterate.T, iterate, precision=precision)
        return 1.5 * iterate - 0.5 * jnp.dot(iterate, square, precision=precision)

    return update


def running_product(rotation, axis, core):
    count, mine = (lax.axis_size(axis), lax.axis_index(axis))
    product = rotation
    steps = 1
    while steps < count:
        received = shifted(halves(product, core)[0], axis, steps)
        earlier = joined(received, swapped(received, "core", 1), core)
        longer = jnp.dot(product, earlier, precision=HIGHEST)
        product = jnp.where(mine >= steps, longer, product)
        steps *= 2
    return product


def per_device(embedding, anchor_rows):
    own_rows = embedding[0]
    width = own_rows.shape[1]
    core = lax.axis_index("core")
    row_index = lax.axis_index("z") * lax.axis_size("core") + core
    positions = anchor_rows - row_index * own_rows.shape[0]
    own_slab = jnp.take(own_rows, positions, axis=0)
    previous_slab = shifted(own_slab, "ver", 1)
    partial_gram = lax.dot_general(
        own_slab, previous_slab, (((0,), (0,)), ((), ())), preferred_element_type=jnp.float32
    )
    cross_gram = summed_over(partial_gram, "z", core)
    frobenius = jnp.sqrt(jnp.sum(cross_gram * cross_gram) + 1e-06)
    iterate = cross_gram / frobenius
    iterate = lax.fori_loop(0, ROUGH_ITERS, newton_update(lax.Precision.HIGH), iterate)
    rotation = lax.fori_loop(ROUGH_ITERS, ITERS, newton_update(HIGHEST), iterate)
    identity_matrix = jnp.eye(width, dtype=jnp.float32)
    rotation = jnp.where(lax.axis_index("ver") == 0, identity_matrix, rotation)
    prefix = running_product(rotation, "ver", core)
    prefix_low = prefix.astype(jnp.bfloat16)
    aligned = jnp.dot(own_rows, prefix_low, preferred_element_type=jnp.float32).astype(jnp.bfloat16)
    return aligned[None]


def solution(mesh):
    versions, rows = mesh.devices.shape
    cores = 2
    split_mesh = Mesh(mesh.devices.reshape(versions, rows // cores, cores), ("ver", "z", "core"))
    row = ("z", "core")
    return jax.shard_map(
        per_device,
        mesh=split_mesh,
        in_specs=(P("ver", row, None), P(row)),
        out_specs=P("ver", row, None),
        check_vma=False,
    )
```

```python
import jax
import jax.numpy as jnp
from jax import lax
from jax.experimental import pallas as pl
from jax.sharding import Mesh, PartitionSpec as P

ITERS = 12
ROUGH_ITERS = 8
HIGHEST = lax.Precision.HIGHEST


def shifted(value, axis, steps):
    count = lax.axis_size(axis)
    return lax.ppermute(value, axis, [(source, source + steps) for source in range(count - steps)])


def swapped(value, axis, mask):
    count = lax.axis_size(axis)
    return lax.ppermute(value, axis, [(source, source ^ mask) for source in range(count)])


def halves(matrix, core):
    half = matrix.shape[0] // 2
    return jnp.where(core == 0, matrix[:half], matrix[half:]), jnp.where(core == 0, matrix[half:], matrix[:half])


def joined(mine, other, core):
    return jnp.where(core == 0, jnp.concatenate([mine, other]), jnp.concatenate([other, mine]))


def summed_over(partial, axis, core):
    mine, other = halves(partial, core)
    mine = mine + swapped(other, "core", 1)
    count = lax.axis_size(axis)
    pieces = mine.reshape(count, mine.shape[0] // count, mine.shape[1])
    reduced = lax.all_to_all(pieces, axis, 0, 0, tiled=False).sum(0)
    copies = jnp.broadcast_to(reduced[None], (count,) + reduced.shape)
    mine = lax.all_to_all(copies, axis, 0, 0, tiled=False).reshape(mine.shape)
    return joined(mine, swapped(mine, "core", 1), core)


def newton_update(precision):
    def update(sweep_index, iterate):
        square = jnp.dot(iterate.T, iterate, precision=precision)
        return 1.5 * iterate - 0.5 * jnp.dot(iterate, square, precision=precision)

    return update


def running_product(rotation, axis, core):
    count, mine = (lax.axis_size(axis), lax.axis_index(axis))
    product = rotation
    steps = 1
    while steps < count:
        received = shifted(halves(product, core)[0], axis, steps)
        earlier = joined(received, swapped(received, "core", 1), core)
        longer = jnp.dot(product, earlier, precision=HIGHEST)
        product = jnp.where(mine >= steps, longer, product)
        steps *= 2
    return product


def aligned_block(rows_ref, prefix_ref, out_ref):
    product = jnp.dot(rows_ref[...], prefix_ref[...], preferred_element_type=jnp.float32)
    out_ref[...] = product.astype(out_ref.dtype)


def aligned_rows(embedding, prefix_low):
    _, rows, width = embedding.shape
    block = 512
    return pl.pallas_call(
        aligned_block,
        grid=(rows // block,),
        in_specs=[
            pl.BlockSpec((None, block, width), lambda i: (0, i, 0)),
            pl.BlockSpec((width, width), lambda i: (0, 0)),
        ],
        out_specs=pl.BlockSpec((None, block, width), lambda i: (0, i, 0)),
        out_shape=jax.ShapeDtypeStruct(embedding.shape, embedding.dtype),
    )(embedding, prefix_low)


def per_device(embedding, anchor_rows):
    own_rows = embedding[0]
    width = own_rows.shape[1]
    core = lax.axis_index("core")
    row_index = lax.axis_index("z") * lax.axis_size("core") + core
    positions = anchor_rows - row_index * own_rows.shape[0]
    own_slab = jnp.take(own_rows, positions, axis=0)
    previous_slab = shifted(own_slab, "ver", 1)
    partial_gram = lax.dot_general(
        own_slab, previous_slab, (((0,), (0,)), ((), ())), preferred_element_type=jnp.float32
    )
    cross_gram = summed_over(partial_gram, "z", core)
    frobenius = jnp.sqrt(jnp.sum(cross_gram * cross_gram) + 1e-06)
    iterate = cross_gram / frobenius
    iterate = lax.fori_loop(0, ROUGH_ITERS, newton_update(lax.Precision.HIGH), iterate)
    rotation = lax.fori_loop(ROUGH_ITERS, ITERS, newton_update(HIGHEST), iterate)
    identity_matrix = jnp.eye(width, dtype=jnp.float32)
    rotation = jnp.where(lax.axis_index("ver") == 0, identity_matrix, rotation)
    prefix = running_product(rotation, "ver", core)
    prefix_low = prefix.astype(jnp.bfloat16)
    return aligned_rows(embedding, prefix_low)


def solution(mesh):
    versions, rows = mesh.devices.shape
    cores = 2
    split_mesh = Mesh(mesh.devices.reshape(versions, rows // cores, cores), ("ver", "z", "core"))
    row = ("z", "core")
    return jax.shard_map(
        per_device,
        mesh=split_mesh,
        in_specs=(P("ver", row, None), P(row)),
        out_specs=P("ver", row, None),
        check_vma=False,
    )
```

```python
import jax
import jax.numpy as jnp
from jax import lax
from jax.experimental import pallas as pl
from jax.sharding import Mesh, PartitionSpec as P

ITERS = 12
ROUGH_ITERS = 8
HIGHEST = lax.Precision.HIGHEST


def shifted(value, axis, steps):
    count = lax.axis_size(axis)
    return lax.ppermute(value, axis, [(source, source + steps) for source in range(count - steps)])


def swapped(value, axis, mask):
    count = lax.axis_size(axis)
    return lax.ppermute(value, axis, [(source, source ^ mask) for source in range(count)])


def halves(matrix, core):
    half = matrix.shape[0] // 2
    return jnp.where(core == 0, matrix[:half], matrix[half:]), jnp.where(core == 0, matrix[half:], matrix[:half])


def joined(mine, other, core):
    return jnp.where(core == 0, jnp.concatenate([mine, other]), jnp.concatenate([other, mine]))


def summed_over(partial, axis, core):
    mine, other = halves(partial, core)
    mine = mine + swapped(other, "core", 1)
    count = lax.axis_size(axis)
    pieces = mine.reshape(count, mine.shape[0] // count, mine.shape[1])
    reduced = lax.all_to_all(pieces, axis, 0, 0, tiled=False).sum(0)
    copies = jnp.broadcast_to(reduced[None], (count,) + reduced.shape)
    mine = lax.all_to_all(copies, axis, 0, 0, tiled=False).reshape(mine.shape)
    return joined(mine, swapped(mine, "core", 1), core)


def newton_update(precision):
    def update(sweep_index, iterate):
        square = jnp.dot(iterate.T, iterate, precision=precision)
        return 1.5 * iterate - 0.5 * jnp.dot(iterate, square, precision=precision)

    return update


def column_half(matrix, core):
    half = matrix.shape[1] // 2
    return jnp.where(core == 0, matrix[:, :half], matrix[:, half:])


def joined_columns(mine, other, core):
    return jnp.where(
        core == 0, jnp.concatenate([mine, other], axis=1), jnp.concatenate([other, mine], axis=1)
    )


def running_product(rotation, axis, core):
    count, mine = (lax.axis_size(axis), lax.axis_index(axis))
    whole = rotation
    own_columns = column_half(rotation, core)
    steps = 1
    while steps < count:
        received = shifted(own_columns, axis, steps)
        longer = jnp.dot(whole, received, precision=HIGHEST)
        own_columns = jnp.where(mine >= steps, longer, own_columns)
        steps *= 2
        if steps < count:
            whole = joined_columns(own_columns, swapped(own_columns, "core", 1), core)
    return own_columns


def aligned_block(rows_ref, prefix_ref, out_ref):
    product = jnp.dot(rows_ref[...], prefix_ref[...], preferred_element_type=jnp.float32)
    out_ref[...] = product.astype(out_ref.dtype)


def aligned_rows(embedding, prefix_low):
    _, rows, width = embedding.shape
    block = 512
    return pl.pallas_call(
        aligned_block,
        grid=(rows // block,),
        in_specs=[
            pl.BlockSpec((None, block, width), lambda i: (0, i, 0)),
            pl.BlockSpec((width, width), lambda i: (0, 0)),
        ],
        out_specs=pl.BlockSpec((None, block, width), lambda i: (0, i, 0)),
        out_shape=jax.ShapeDtypeStruct(embedding.shape, embedding.dtype),
    )(embedding, prefix_low)


def per_device(embedding, anchor_rows):
    own_rows = embedding[0]
    width = own_rows.shape[1]
    core = lax.axis_index("core")
    row_index = lax.axis_index("z") * lax.axis_size("core") + core
    positions = anchor_rows - row_index * own_rows.shape[0]
    own_slab = jnp.take(own_rows, positions, axis=0)
    previous_slab = shifted(own_slab, "ver", 1)
    partial_gram = lax.dot_general(
        own_slab, previous_slab, (((0,), (0,)), ((), ())), preferred_element_type=jnp.float32
    )
    cross_gram = summed_over(partial_gram, "z", core)
    frobenius = jnp.sqrt(jnp.sum(cross_gram * cross_gram) + 1e-06)
    iterate = cross_gram / frobenius
    iterate = lax.fori_loop(0, ROUGH_ITERS, newton_update(lax.Precision.HIGH), iterate)
    rotation = lax.fori_loop(ROUGH_ITERS, ITERS, newton_update(HIGHEST), iterate)
    identity_matrix = jnp.eye(width, dtype=jnp.float32)
    rotation = jnp.where(lax.axis_index("ver") == 0, identity_matrix, rotation)
    own_low = running_product(rotation, "ver", core).astype(jnp.bfloat16)
    prefix_low = joined_columns(own_low, swapped(own_low, "core", 1), core)
    return aligned_rows(embedding, prefix_low)


def solution(mesh):
    versions, rows = mesh.devices.shape
    cores = 2
    split_mesh = Mesh(mesh.devices.reshape(versions, rows // cores, cores), ("ver", "z", "core"))
    row = ("z", "core")
    return jax.shard_map(
        per_device,
        mesh=split_mesh,
        in_specs=(P("ver", row, None), P(row)),
        out_specs=P("ver", row, None),
        check_vma=False,
    )
```

```python
import jax
import jax.numpy as jnp
from jax import lax
from jax.experimental import pallas as pl
from jax.sharding import Mesh, PartitionSpec as P

ITERS = 12
ROUGH_ITERS = 10
HIGHEST = lax.Precision.HIGHEST


def shifted(value, axis, steps):
    count = lax.axis_size(axis)
    return lax.ppermute(value, axis, [(source, source + steps) for source in range(count - steps)])


def swapped(value, axis, mask):
    count = lax.axis_size(axis)
    return lax.ppermute(value, axis, [(source, source ^ mask) for source in range(count)])


def halves(matrix, core):
    half = matrix.shape[0] // 2
    return jnp.where(core == 0, matrix[:half], matrix[half:]), jnp.where(core == 0, matrix[half:], matrix[:half])


def joined(mine, other, core):
    return jnp.where(core == 0, jnp.concatenate([mine, other]), jnp.concatenate([other, mine]))


def summed_over(partial, axis, core):
    mine, other = halves(partial, core)
    mine = mine + swapped(other, "core", 1)
    count = lax.axis_size(axis)
    pieces = mine.reshape(count, mine.shape[0] // count, mine.shape[1])
    reduced = lax.all_to_all(pieces, axis, 0, 0, tiled=False).sum(0)
    copies = jnp.broadcast_to(reduced[None], (count,) + reduced.shape)
    mine = lax.all_to_all(copies, axis, 0, 0, tiled=False).reshape(mine.shape)
    return joined(mine, swapped(mine, "core", 1), core)


def newton_update(precision):
    def update(sweep_index, iterate):
        square = jnp.dot(iterate.T, iterate, precision=precision)
        return 1.5 * iterate - 0.5 * jnp.dot(iterate, square, precision=precision)

    return update


def column_half(matrix, core):
    half = matrix.shape[1] // 2
    return jnp.where(core == 0, matrix[:, :half], matrix[:, half:])


def joined_columns(mine, other, core):
    return jnp.where(
        core == 0, jnp.concatenate([mine, other], axis=1), jnp.concatenate([other, mine], axis=1)
    )


def running_product(rotation, axis, core):
    count, mine = (lax.axis_size(axis), lax.axis_index(axis))
    whole = rotation
    own_columns = column_half(rotation, core)
    steps = 1
    while steps < count:
        received = shifted(own_columns, axis, steps)
        longer = jnp.dot(whole, received, precision=HIGHEST)
        own_columns = jnp.where(mine >= steps, longer, own_columns)
        steps *= 2
        if steps < count:
            whole = joined_columns(own_columns, swapped(own_columns, "core", 1), core)
    return own_columns


def aligned_block(rows_ref, prefix_ref, out_ref):
    product = jnp.dot(rows_ref[...], prefix_ref[...], preferred_element_type=jnp.float32)
    out_ref[...] = product.astype(out_ref.dtype)


def aligned_rows(embedding, prefix_low):
    _, rows, width = embedding.shape
    block = 512
    return pl.pallas_call(
        aligned_block,
        grid=(rows // block,),
        in_specs=[
            pl.BlockSpec((None, block, width), lambda i: (0, i, 0)),
            pl.BlockSpec((width, width), lambda i: (0, 0)),
        ],
        out_specs=pl.BlockSpec((None, block, width), lambda i: (0, i, 0)),
        out_shape=jax.ShapeDtypeStruct(embedding.shape, embedding.dtype),
    )(embedding, prefix_low)


def per_device(embedding, anchor_rows):
    own_rows = embedding[0]
    width = own_rows.shape[1]
    core = lax.axis_index("core")
    row_index = lax.axis_index("z") * lax.axis_size("core") + core
    positions = anchor_rows - row_index * own_rows.shape[0]
    own_slab = jnp.take(own_rows, positions, axis=0)
    previous_slab = shifted(own_slab, "ver", 1)
    partial_gram = lax.dot_general(
        own_slab, previous_slab, (((0,), (0,)), ((), ())), preferred_element_type=jnp.float32
    )
    cross_gram = summed_over(partial_gram, "z", core)
    frobenius = jnp.sqrt(jnp.sum(cross_gram * cross_gram) + 1e-06)
    iterate = cross_gram / frobenius
    iterate = lax.fori_loop(0, ROUGH_ITERS, newton_update(lax.Precision.HIGH), iterate)
    rotation = lax.fori_loop(ROUGH_ITERS, ITERS, newton_update(HIGHEST), iterate)
    identity_matrix = jnp.eye(width, dtype=jnp.float32)
    rotation = jnp.where(lax.axis_index("ver") == 0, identity_matrix, rotation)
    own_low = running_product(rotation, "ver", core).astype(jnp.bfloat16)
    prefix_low = joined_columns(own_low, swapped(own_low, "core", 1), core)
    return aligned_rows(embedding, prefix_low)


def solution(mesh):
    versions, rows = mesh.devices.shape
    cores = 2
    split_mesh = Mesh(mesh.devices.reshape(versions, rows // cores, cores), ("ver", "z", "core"))
    row = ("z", "core")
    return jax.shard_map(
        per_device,
        mesh=split_mesh,
        in_specs=(P("ver", row, None), P(row)),
        out_specs=P("ver", row, None),
        check_vma=False,
    )
```

```python
import jax
import jax.numpy as jnp
from jax import lax
from jax.experimental import pallas as pl
from jax.sharding import Mesh, PartitionSpec as P

ITERS = 12
ROUGH_ITERS = 10
HIGHEST = lax.Precision.HIGHEST


def shifted(value, axis, steps):
    count = lax.axis_size(axis)
    return lax.ppermute(value, axis, [(source, source + steps) for source in range(count - steps)])


def swapped(value, axis, mask):
    count = lax.axis_size(axis)
    return lax.ppermute(value, axis, [(source, source ^ mask) for source in range(count)])


def halves(matrix, core):
    half = matrix.shape[0] // 2
    return jnp.where(core == 0, matrix[:half], matrix[half:]), jnp.where(core == 0, matrix[half:], matrix[:half])


def joined(mine, other, core):
    return jnp.where(core == 0, jnp.concatenate([mine, other]), jnp.concatenate([other, mine]))


def summed_over(partial, axis, core):
    mine, other = halves(partial, core)
    mine = mine + swapped(other, "core", 1)
    count = lax.axis_size(axis)
    pieces = mine.reshape(count, mine.shape[0] // count, mine.shape[1])
    reduced = lax.all_to_all(pieces, axis, 0, 0, tiled=False).sum(0)
    copies = jnp.broadcast_to(reduced[None], (count,) + reduced.shape)
    mine = lax.all_to_all(copies, axis, 0, 0, tiled=False).reshape(mine.shape)
    return joined(mine, swapped(mine, "core", 1), core)


def newton_update(precision):
    def update(sweep_index, iterate):
        square = jnp.dot(iterate.T, iterate, precision=precision)
        return 1.5 * iterate - 0.5 * jnp.dot(iterate, square, precision=precision)

    return update


def column_half(matrix, core):
    half = matrix.shape[1] // 2
    return jnp.where(core == 0, matrix[:, :half], matrix[:, half:])


def joined_columns(mine, other, core):
    return jnp.where(
        core == 0, jnp.concatenate([mine, other], axis=1), jnp.concatenate([other, mine], axis=1)
    )


def running_product(rotation, axis, core):
    count, mine = (lax.axis_size(axis), lax.axis_index(axis))
    whole = rotation
    own_columns = column_half(rotation, core)
    steps = 1
    while steps < count:
        received = shifted(own_columns, axis, steps)
        longer = jnp.dot(whole, received, precision=HIGHEST)
        own_columns = jnp.where(mine >= steps, longer, own_columns)
        steps *= 2
        if steps < count:
            whole = joined_columns(own_columns, swapped(own_columns, "core", 1), core)
    return own_columns


def aligned_block(rows_ref, prefix_ref, out_ref):
    product = jnp.dot(rows_ref[...], prefix_ref[...], preferred_element_type=jnp.float32)
    out_ref[...] = product.astype(out_ref.dtype)


def aligned_rows(embedding, prefix_low):
    _, rows, width = embedding.shape
    block = 512
    return pl.pallas_call(
        aligned_block,
        grid=(rows // block,),
        in_specs=[
            pl.BlockSpec((None, block, width), lambda i: (0, i, 0)),
            pl.BlockSpec((width, width), lambda i: (0, 0)),
        ],
        out_specs=pl.BlockSpec((None, block, width), lambda i: (0, i, 0)),
        out_shape=jax.ShapeDtypeStruct(embedding.shape, embedding.dtype),
    )(embedding, prefix_low)


def per_device(embedding, anchor_rows):
    own_rows = embedding[0]
    width = own_rows.shape[1]
    core = lax.axis_index("core")
    row_index = lax.axis_index("z") * lax.axis_size("core") + core
    positions = anchor_rows - row_index * own_rows.shape[0]
    own_slab = jnp.take(own_rows, positions, axis=0)
    half = width // 2
    column_grams = []
    for start in (0, half):
        previous_columns = shifted(own_slab[:, start : start + half], "ver", 1)
        partial_gram = lax.dot_general(
            own_slab, previous_columns, (((0,), (0,)), ((), ())), preferred_element_type=jnp.float32
        )
        column_grams.append(summed_over(partial_gram, "z", core))
    cross_gram = jnp.concatenate(column_grams, axis=1)
    frobenius = jnp.sqrt(jnp.sum(cross_gram * cross_gram) + 1e-06)
    iterate = cross_gram / frobenius
    iterate = lax.fori_loop(0, ROUGH_ITERS, newton_update(lax.Precision.HIGH), iterate)
    rotation = lax.fori_loop(ROUGH_ITERS, ITERS, newton_update(HIGHEST), iterate)
    identity_matrix = jnp.eye(width, dtype=jnp.float32)
    rotation = jnp.where(lax.axis_index("ver") == 0, identity_matrix, rotation)
    own_low = running_product(rotation, "ver", core).astype(jnp.bfloat16)
    prefix_low = joined_columns(own_low, swapped(own_low, "core", 1), core)
    return aligned_rows(embedding, prefix_low)


def solution(mesh):
    versions, rows = mesh.devices.shape
    cores = 2
    split_mesh = Mesh(mesh.devices.reshape(versions, rows // cores, cores), ("ver", "z", "core"))
    row = ("z", "core")
    return jax.shard_map(
        per_device,
        mesh=split_mesh,
        in_specs=(P("ver", row, None), P(row)),
        out_specs=P("ver", row, None),
        check_vma=False,
    )
```

```python
import jax
import jax.numpy as jnp
from jax import lax
from jax.experimental import pallas as pl
from jax.sharding import Mesh, PartitionSpec as P

ITERS = 12
ROUGH_ITERS = 10
HIGHEST = lax.Precision.HIGHEST


def shifted(value, axis, steps):
    count = lax.axis_size(axis)
    return lax.ppermute(value, axis, [(source, source + steps) for source in range(count - steps)])


def swapped(value, axis, mask):
    count = lax.axis_size(axis)
    return lax.ppermute(value, axis, [(source, source ^ mask) for source in range(count)])


def halves(matrix, core):
    half = matrix.shape[0] // 2
    return jnp.where(core == 0, matrix[:half], matrix[half:]), jnp.where(core == 0, matrix[half:], matrix[:half])


def joined(mine, other, core):
    return jnp.where(core == 0, jnp.concatenate([mine, other]), jnp.concatenate([other, mine]))


def summed_over(partial, axis, core):
    mine, other = halves(partial, core)
    mine = mine + swapped(other, "core", 1)
    count = lax.axis_size(axis)
    pieces = mine.reshape(count, mine.shape[0] // count, mine.shape[1])
    reduced = lax.all_to_all(pieces, axis, 0, 0, tiled=False).sum(0)
    copies = jnp.broadcast_to(reduced[None], (count,) + reduced.shape)
    mine = lax.all_to_all(copies, axis, 0, 0, tiled=False).reshape(mine.shape)
    return joined(mine, swapped(mine, "core", 1), core)


def newton_update(precision):
    def update(sweep_index, iterate):
        square = jnp.dot(iterate.T, iterate, precision=precision)
        return 1.5 * iterate - 0.5 * jnp.dot(iterate, square, precision=precision)

    return update


def column_half(matrix, core):
    half = matrix.shape[1] // 2
    return jnp.where(core == 0, matrix[:, :half], matrix[:, half:])


def joined_columns(mine, other, core):
    return jnp.where(
        core == 0, jnp.concatenate([mine, other], axis=1), jnp.concatenate([other, mine], axis=1)
    )


def running_product(rotation, axis, core):
    count, mine = (lax.axis_size(axis), lax.axis_index(axis))
    whole = rotation
    own_columns = column_half(rotation, core)
    steps = 1
    while steps < count:
        received = shifted(own_columns, axis, steps)
        longer = jnp.dot(whole, received, precision=HIGHEST)
        own_columns = jnp.where(mine >= steps, longer, own_columns)
        steps *= 2
        if steps < count:
            whole = joined_columns(own_columns, swapped(own_columns, "core", 1), core)
    return own_columns


def aligned_block(rows_ref, prefix_ref, out_ref):
    product = jnp.dot(rows_ref[...], prefix_ref[...], preferred_element_type=jnp.float32)
    out_ref[...] = product.astype(out_ref.dtype)


def aligned_rows(embedding, prefix_low):
    _, rows, width = embedding.shape
    block = 512
    return pl.pallas_call(
        aligned_block,
        grid=(rows // block,),
        in_specs=[
            pl.BlockSpec((None, block, width), lambda i: (0, i, 0)),
            pl.BlockSpec((width, width), lambda i: (0, 0)),
        ],
        out_specs=pl.BlockSpec((None, block, width), lambda i: (0, i, 0)),
        out_shape=jax.ShapeDtypeStruct(embedding.shape, embedding.dtype),
    )(embedding, prefix_low)


def per_device(embedding, anchor_rows):
    own_rows = embedding[0]
    width = own_rows.shape[1]
    core = lax.axis_index("core")
    row_index = lax.axis_index("z") * lax.axis_size("core") + core
    positions = anchor_rows - row_index * own_rows.shape[0]
    picks = (positions[:, None] == jnp.arange(own_rows.shape[0], dtype=positions.dtype)[None, :])
    own_slab = jnp.dot(
        picks.astype(own_rows.dtype), own_rows, preferred_element_type=jnp.float32
    ).astype(own_rows.dtype)
    previous_slab = shifted(own_slab, "ver", 1)
    partial_gram = lax.dot_general(
        own_slab, previous_slab, (((0,), (0,)), ((), ())), preferred_element_type=jnp.float32
    )
    cross_gram = summed_over(partial_gram, "z", core)
    frobenius = jnp.sqrt(jnp.sum(cross_gram * cross_gram) + 1e-06)
    iterate = cross_gram / frobenius
    iterate = lax.fori_loop(0, ROUGH_ITERS, newton_update(lax.Precision.HIGH), iterate)
    rotation = lax.fori_loop(ROUGH_ITERS, ITERS, newton_update(HIGHEST), iterate)
    identity_matrix = jnp.eye(width, dtype=jnp.float32)
    rotation = jnp.where(lax.axis_index("ver") == 0, identity_matrix, rotation)
    own_low = running_product(rotation, "ver", core).astype(jnp.bfloat16)
    prefix_low = joined_columns(own_low, swapped(own_low, "core", 1), core)
    return aligned_rows(embedding, prefix_low)


def solution(mesh):
    versions, rows = mesh.devices.shape
    cores = 2
    split_mesh = Mesh(mesh.devices.reshape(versions, rows // cores, cores), ("ver", "z", "core"))
    row = ("z", "core")
    return jax.shard_map(
        per_device,
        mesh=split_mesh,
        in_specs=(P("ver", row, None), P(row)),
        out_specs=P("ver", row, None),
        check_vma=False,
    )
```

```python
import jax
import jax.numpy as jnp
from jax import lax
from jax.experimental import pallas as pl
from jax.sharding import Mesh, PartitionSpec as P

ITERS = 12
ROUGH_ITERS = 10
HIGHEST = lax.Precision.HIGHEST


def shifted(value, axis, steps):
    count = lax.axis_size(axis)
    return lax.ppermute(value, axis, [(source, source + steps) for source in range(count - steps)])


def swapped(value, axis, mask):
    count = lax.axis_size(axis)
    return lax.ppermute(value, axis, [(source, source ^ mask) for source in range(count)])


def halves(matrix, core):
    half = matrix.shape[0] // 2
    return jnp.where(core == 0, matrix[:half], matrix[half:]), jnp.where(core == 0, matrix[half:], matrix[:half])


def joined(mine, other, core):
    return jnp.where(core == 0, jnp.concatenate([mine, other]), jnp.concatenate([other, mine]))


def summed_over(partial, axis, core):
    mine, other = halves(partial, core)
    mine = mine + swapped(other, "core", 1)
    count = lax.axis_size(axis)
    pieces = mine.reshape(count, mine.shape[0] // count, mine.shape[1])
    reduced = lax.all_to_all(pieces, axis, 0, 0, tiled=False).sum(0)
    copies = jnp.broadcast_to(reduced[None], (count,) + reduced.shape)
    mine = lax.all_to_all(copies, axis, 0, 0, tiled=False).reshape(mine.shape)
    return joined(mine, swapped(mine, "core", 1), core)


def newton_update(precision):
    def update(sweep_index, iterate):
        square = jnp.dot(iterate.T, iterate, precision=precision)
        return 1.5 * iterate - 0.5 * jnp.dot(iterate, square, precision=precision)

    return update


def column_half(matrix, core):
    half = matrix.shape[1] // 2
    return jnp.where(core == 0, matrix[:, :half], matrix[:, half:])


def joined_columns(mine, other, core):
    return jnp.where(
        core == 0, jnp.concatenate([mine, other], axis=1), jnp.concatenate([other, mine], axis=1)
    )


def running_product(rotation, axis, core):
    count, mine = (lax.axis_size(axis), lax.axis_index(axis))
    whole = rotation
    own_columns = column_half(rotation, core)
    steps = 1
    while steps < count:
        received = shifted(own_columns, axis, steps)
        longer = jnp.dot(whole, received, precision=HIGHEST)
        own_columns = jnp.where(mine >= steps, longer, own_columns)
        steps *= 2
        if steps < count:
            whole = joined_columns(own_columns, swapped(own_columns, "core", 1), core)
    return own_columns


def aligned_block(rows_ref, prefix_ref, out_ref):
    product = jnp.dot(rows_ref[...], prefix_ref[...], preferred_element_type=jnp.float32)
    out_ref[...] = product.astype(out_ref.dtype)


def aligned_rows(embedding, prefix_low):
    _, rows, width = embedding.shape
    block = 256
    return pl.pallas_call(
        aligned_block,
        grid=(rows // block,),
        in_specs=[
            pl.BlockSpec((None, block, width), lambda i: (0, i, 0)),
            pl.BlockSpec((width, width), lambda i: (0, 0)),
        ],
        out_specs=pl.BlockSpec((None, block, width), lambda i: (0, i, 0)),
        out_shape=jax.ShapeDtypeStruct(embedding.shape, embedding.dtype),
    )(embedding, prefix_low)


def per_device(embedding, anchor_rows):
    own_rows = embedding[0]
    width = own_rows.shape[1]
    core = lax.axis_index("core")
    row_index = lax.axis_index("z") * lax.axis_size("core") + core
    positions = anchor_rows - row_index * own_rows.shape[0]
    picks = (positions[:, None] == jnp.arange(own_rows.shape[0], dtype=positions.dtype)[None, :])
    own_slab = jnp.dot(
        picks.astype(own_rows.dtype), own_rows, preferred_element_type=jnp.float32
    ).astype(own_rows.dtype)
    previous_slab = shifted(own_slab, "ver", 1)
    partial_gram = lax.dot_general(
        own_slab, previous_slab, (((0,), (0,)), ((), ())), preferred_element_type=jnp.float32
    )
    cross_gram = summed_over(partial_gram, "z", core)
    frobenius = jnp.sqrt(jnp.sum(cross_gram * cross_gram) + 1e-06)
    iterate = cross_gram / frobenius
    iterate = lax.fori_loop(0, ROUGH_ITERS, newton_update(lax.Precision.HIGH), iterate)
    rotation = lax.fori_loop(ROUGH_ITERS, ITERS, newton_update(HIGHEST), iterate)
    identity_matrix = jnp.eye(width, dtype=jnp.float32)
    rotation = jnp.where(lax.axis_index("ver") == 0, identity_matrix, rotation)
    own_low = running_product(rotation, "ver", core).astype(jnp.bfloat16)
    prefix_low = joined_columns(own_low, swapped(own_low, "core", 1), core)
    return aligned_rows(embedding, prefix_low)


def solution(mesh):
    versions, rows = mesh.devices.shape
    cores = 2
    split_mesh = Mesh(mesh.devices.reshape(versions, rows // cores, cores), ("ver", "z", "core"))
    row = ("z", "core")
    return jax.shard_map(
        per_device,
        mesh=split_mesh,
        in_specs=(P("ver", row, None), P(row)),
        out_specs=P("ver", row, None),
        check_vma=False,
    )
```

```python
import jax
import jax.numpy as jnp
from jax import lax
from jax.experimental import pallas as pl
from jax.sharding import Mesh, PartitionSpec as P

ITERS = 12
ROUGH_ITERS = 10
HIGHEST = lax.Precision.HIGHEST


def shifted(value, axis, steps):
    count = lax.axis_size(axis)
    return lax.ppermute(value, axis, [(source, source + steps) for source in range(count - steps)])


def swapped(value, axis, mask):
    count = lax.axis_size(axis)
    return lax.ppermute(value, axis, [(source, source ^ mask) for source in range(count)])


def halves(matrix, core):
    half = matrix.shape[0] // 2
    return jnp.where(core == 0, matrix[:half], matrix[half:]), jnp.where(core == 0, matrix[half:], matrix[:half])


def joined(mine, other, core):
    return jnp.where(core == 0, jnp.concatenate([mine, other]), jnp.concatenate([other, mine]))


def summed_over(partial, axis, core):
    mine, other = halves(partial, core)
    mine = mine + swapped(other, "core", 1)
    count = lax.axis_size(axis)
    pieces = mine.reshape(count, mine.shape[0] // count, mine.shape[1])
    reduced = lax.all_to_all(pieces, axis, 0, 0, tiled=False).sum(0)
    copies = jnp.broadcast_to(reduced[None], (count,) + reduced.shape)
    mine = lax.all_to_all(copies, axis, 0, 0, tiled=False).reshape(mine.shape)
    return joined(mine, swapped(mine, "core", 1), core)


def newton_update(precision):
    def update(sweep_index, iterate):
        square = jnp.dot(iterate.T, iterate, precision=precision)
        return 1.5 * iterate - 0.5 * jnp.dot(iterate, square, precision=precision)

    return update


def column_half(matrix, core):
    half = matrix.shape[1] // 2
    return jnp.where(core == 0, matrix[:, :half], matrix[:, half:])


def joined_columns(mine, other, core):
    return jnp.where(
        core == 0, jnp.concatenate([mine, other], axis=1), jnp.concatenate([other, mine], axis=1)
    )


def running_product(rotation, axis, core):
    count, mine = (lax.axis_size(axis), lax.axis_index(axis))
    whole = rotation
    own_columns = column_half(rotation, core)
    steps = 1
    while steps < count:
        received = shifted(own_columns, axis, steps)
        longer = jnp.dot(whole, received, precision=HIGHEST)
        own_columns = jnp.where(mine >= steps, longer, own_columns)
        steps *= 2
        if steps < count:
            whole = joined_columns(own_columns, swapped(own_columns, "core", 1), core)
    return own_columns


def aligned_block(rows_ref, prefix_ref, out_ref):
    product = jnp.dot(rows_ref[...], prefix_ref[...], preferred_element_type=jnp.float32)
    out_ref[...] = product.astype(out_ref.dtype)


def aligned_rows(embedding, prefix_low):
    _, rows, width = embedding.shape
    block = 1024
    return pl.pallas_call(
        aligned_block,
        grid=(rows // block,),
        in_specs=[
            pl.BlockSpec((None, block, width), lambda i: (0, i, 0)),
            pl.BlockSpec((width, width), lambda i: (0, 0)),
        ],
        out_specs=pl.BlockSpec((None, block, width), lambda i: (0, i, 0)),
        out_shape=jax.ShapeDtypeStruct(embedding.shape, embedding.dtype),
    )(embedding, prefix_low)


def per_device(embedding, anchor_rows):
    own_rows = embedding[0]
    width = own_rows.shape[1]
    core = lax.axis_index("core")
    row_index = lax.axis_index("z") * lax.axis_size("core") + core
    positions = anchor_rows - row_index * own_rows.shape[0]
    picks = (positions[:, None] == jnp.arange(own_rows.shape[0], dtype=positions.dtype)[None, :])
    own_slab = jnp.dot(
        picks.astype(own_rows.dtype), own_rows, preferred_element_type=jnp.float32
    ).astype(own_rows.dtype)
    previous_slab = shifted(own_slab, "ver", 1)
    partial_gram = lax.dot_general(
        own_slab, previous_slab, (((0,), (0,)), ((), ())), preferred_element_type=jnp.float32
    )
    cross_gram = summed_over(partial_gram, "z", core)
    frobenius = jnp.sqrt(jnp.sum(cross_gram * cross_gram) + 1e-06)
    iterate = cross_gram / frobenius
    iterate = lax.fori_loop(0, ROUGH_ITERS, newton_update(lax.Precision.HIGH), iterate)
    rotation = lax.fori_loop(ROUGH_ITERS, ITERS, newton_update(HIGHEST), iterate)
    identity_matrix = jnp.eye(width, dtype=jnp.float32)
    rotation = jnp.where(lax.axis_index("ver") == 0, identity_matrix, rotation)
    own_low = running_product(rotation, "ver", core).astype(jnp.bfloat16)
    prefix_low = joined_columns(own_low, swapped(own_low, "core", 1), core)
    return aligned_rows(embedding, prefix_low)


def solution(mesh):
    versions, rows = mesh.devices.shape
    cores = 2
    split_mesh = Mesh(mesh.devices.reshape(versions, rows // cores, cores), ("ver", "z", "core"))
    row = ("z", "core")
    return jax.shard_map(
        per_device,
        mesh=split_mesh,
        in_specs=(P("ver", row, None), P(row)),
        out_specs=P("ver", row, None),
        check_vma=False,
    )
```

```python
import jax
import jax.numpy as jnp
from jax import lax
from jax.experimental import pallas as pl
from jax.experimental.pallas import tpu as pltpu
from jax.sharding import Mesh, PartitionSpec as P

ITERS = 12
ROUGH_ITERS = 10
HIGHEST = lax.Precision.HIGHEST


def shifted(value, axis, steps):
    count = lax.axis_size(axis)
    return lax.ppermute(value, axis, [(source, source + steps) for source in range(count - steps)])


def swapped(value, axis, mask):
    count = lax.axis_size(axis)
    return lax.ppermute(value, axis, [(source, source ^ mask) for source in range(count)])


def halves(matrix, core):
    half = matrix.shape[0] // 2
    return jnp.where(core == 0, matrix[:half], matrix[half:]), jnp.where(core == 0, matrix[half:], matrix[:half])


def joined(mine, other, core):
    return jnp.where(core == 0, jnp.concatenate([mine, other]), jnp.concatenate([other, mine]))


def summed_over(partial, axis, core):
    mine, other = halves(partial, core)
    mine = mine + swapped(other, "core", 1)
    count = lax.axis_size(axis)
    pieces = mine.reshape(count, mine.shape[0] // count, mine.shape[1])
    reduced = lax.all_to_all(pieces, axis, 0, 0, tiled=False).sum(0)
    copies = jnp.broadcast_to(reduced[None], (count,) + reduced.shape)
    mine = lax.all_to_all(copies, axis, 0, 0, tiled=False).reshape(mine.shape)
    return joined(mine, swapped(mine, "core", 1), core)


def newton_update(precision):
    def update(sweep_index, iterate):
        square = jnp.dot(iterate.T, iterate, precision=precision)
        return 1.5 * iterate - 0.5 * jnp.dot(iterate, square, precision=precision)

    return update


def column_half(matrix, core):
    half = matrix.shape[1] // 2
    return jnp.where(core == 0, matrix[:, :half], matrix[:, half:])


def joined_columns(mine, other, core):
    return jnp.where(
        core == 0, jnp.concatenate([mine, other], axis=1), jnp.concatenate([other, mine], axis=1)
    )


def running_product(rotation, axis, core):
    count, mine = (lax.axis_size(axis), lax.axis_index(axis))
    whole = rotation
    own_columns = column_half(rotation, core)
    steps = 1
    while steps < count:
        received = shifted(own_columns, axis, steps)
        longer = jnp.dot(whole, received, precision=HIGHEST)
        own_columns = jnp.where(mine >= steps, longer, own_columns)
        steps *= 2
        if steps < count:
            whole = joined_columns(own_columns, swapped(own_columns, "core", 1), core)
    return own_columns


def aligned_block(core_ref, rows_ref, own_ref, other_ref, out_ref):
    half = own_ref.shape[1]
    rows = rows_ref[...]

    def store(left_ref, right_ref):
        out_ref[:, :half] = jnp.dot(rows, left_ref[...], preferred_element_type=jnp.float32).astype(out_ref.dtype)
        out_ref[:, half:] = jnp.dot(rows, right_ref[...], preferred_element_type=jnp.float32).astype(out_ref.dtype)

    @pl.when(core_ref[0] == 0)
    def _():
        store(own_ref, other_ref)

    @pl.when(core_ref[0] != 0)
    def _():
        store(other_ref, own_ref)


def aligned_rows(embedding, own_low, other_low, core):
    _, rows, width = embedding.shape
    half = own_low.shape[1]
    block = 512
    return pl.pallas_call(
        aligned_block,
        grid_spec=pltpu.PrefetchScalarGridSpec(
            num_scalar_prefetch=1,
            grid=(rows // block,),
            in_specs=[
                pl.BlockSpec((None, block, width), lambda i, c: (0, i, 0)),
                pl.BlockSpec((width, half), lambda i, c: (0, 0)),
                pl.BlockSpec((width, half), lambda i, c: (0, 0)),
            ],
            out_specs=pl.BlockSpec((None, block, width), lambda i, c: (0, i, 0)),
        ),
        out_shape=jax.ShapeDtypeStruct(embedding.shape, embedding.dtype),
    )(jnp.reshape(core, (1,)).astype(jnp.int32), embedding, own_low, other_low)


def per_device(embedding, anchor_rows):
    own_rows = embedding[0]
    width = own_rows.shape[1]
    core = lax.axis_index("core")
    row_index = lax.axis_index("z") * lax.axis_size("core") + core
    positions = anchor_rows - row_index * own_rows.shape[0]
    picks = (positions[:, None] == jnp.arange(own_rows.shape[0], dtype=positions.dtype)[None, :])
    own_slab = jnp.dot(
        picks.astype(own_rows.dtype), own_rows, preferred_element_type=jnp.float32
    ).astype(own_rows.dtype)
    previous_slab = shifted(own_slab, "ver", 1)
    partial_gram = lax.dot_general(
        own_slab, previous_slab, (((0,), (0,)), ((), ())), preferred_element_type=jnp.float32
    )
    cross_gram = summed_over(partial_gram, "z", core)
    frobenius = jnp.sqrt(jnp.sum(cross_gram * cross_gram) + 1e-06)
    iterate = cross_gram / frobenius
    iterate = lax.fori_loop(0, ROUGH_ITERS, newton_update(lax.Precision.HIGH), iterate)
    rotation = lax.fori_loop(ROUGH_ITERS, ITERS, newton_update(HIGHEST), iterate)
    identity_matrix = jnp.eye(width, dtype=jnp.float32)
    rotation = jnp.where(lax.axis_index("ver") == 0, identity_matrix, rotation)
    own_low = running_product(rotation, "ver", core).astype(jnp.bfloat16)
    return aligned_rows(embedding, own_low, swapped(own_low, "core", 1), core)


def solution(mesh):
    versions, rows = mesh.devices.shape
    cores = 2
    split_mesh = Mesh(mesh.devices.reshape(versions, rows // cores, cores), ("ver", "z", "core"))
    row = ("z", "core")
    return jax.shard_map(
        per_device,
        mesh=split_mesh,
        in_specs=(P("ver", row, None), P(row)),
        out_specs=P("ver", row, None),
        check_vma=False,
    )
```

```python
import jax
import jax.numpy as jnp
from jax import lax
from jax.experimental import pallas as pl
from jax.sharding import Mesh, PartitionSpec as P

ITERS = 12
ROUGH_ITERS = 10
HIGHEST = lax.Precision.HIGHEST


def shifted(value, axis, steps):
    count = lax.axis_size(axis)
    return lax.ppermute(value, axis, [(source, source + steps) for source in range(count - steps)])


def swapped(value, axis, mask):
    count = lax.axis_size(axis)
    return lax.ppermute(value, axis, [(source, source ^ mask) for source in range(count)])


def halves(matrix, core):
    half = matrix.shape[0] // 2
    return jnp.where(core == 0, matrix[:half], matrix[half:]), jnp.where(core == 0, matrix[half:], matrix[:half])


def joined(mine, other, core):
    return jnp.where(core == 0, jnp.concatenate([mine, other]), jnp.concatenate([other, mine]))


def summed_over(partial, axis, core):
    mine, other = halves(partial, core)
    mine = mine + swapped(other, "core", 1)
    count = lax.axis_size(axis)
    pieces = mine.reshape(count, mine.shape[0] // count, mine.shape[1])
    reduced = lax.all_to_all(pieces, axis, 0, 0, tiled=False).sum(0)
    copies = jnp.broadcast_to(reduced[None], (count,) + reduced.shape)
    mine = lax.all_to_all(copies, axis, 0, 0, tiled=False).reshape(mine.shape)
    return joined(mine, swapped(mine, "core", 1), core)


def newton_update(precision):
    def update(sweep_index, iterate):
        square = jnp.dot(iterate.T, iterate, precision=precision)
        return 1.5 * iterate - 0.5 * jnp.dot(iterate, square, precision=precision)

    return update


def column_half(matrix, core):
    half = matrix.shape[1] // 2
    return jnp.where(core == 0, matrix[:, :half], matrix[:, half:])


def joined_columns(mine, other, core):
    return jnp.where(
        core == 0, jnp.concatenate([mine, other], axis=1), jnp.concatenate([other, mine], axis=1)
    )


def running_product(rotation, axis, core):
    count, mine = (lax.axis_size(axis), lax.axis_index(axis))
    whole = rotation
    own_columns = column_half(rotation, core)
    steps = 1
    while steps < count:
        received = shifted(own_columns, axis, steps)
        longer = jnp.dot(whole, received, precision=HIGHEST)
        own_columns = jnp.where(mine >= steps, longer, own_columns)
        steps *= 2
        if steps < count:
            whole = joined_columns(own_columns, swapped(own_columns, "core", 1), core)
    return own_columns


def aligned_block(rows_ref, prefix_ref, out_ref):
    product = jnp.dot(rows_ref[...], prefix_ref[...], preferred_element_type=jnp.float32)
    out_ref[...] = product.astype(out_ref.dtype)


def aligned_rows(embedding, prefix_low):
    _, rows, width = embedding.shape
    block = 512
    return pl.pallas_call(
        aligned_block,
        grid=(rows // block,),
        in_specs=[
            pl.BlockSpec((None, block, width), lambda i: (0, i, 0)),
            pl.BlockSpec((width, width), lambda i: (0, 0)),
        ],
        out_specs=pl.BlockSpec((None, block, width), lambda i: (0, i, 0)),
        out_shape=jax.ShapeDtypeStruct(embedding.shape, embedding.dtype),
    )(embedding, prefix_low)


def per_device(embedding, anchor_rows):
    own_rows = embedding[0]
    width = own_rows.shape[1]
    core = lax.axis_index("core")
    row_index = lax.axis_index("z") * lax.axis_size("core") + core
    positions = anchor_rows - row_index * own_rows.shape[0]
    table_index = jnp.arange(own_rows.shape[0], dtype=positions.dtype)[None, :]
    own_parts, previous_parts = [], []
    for part in jnp.split(positions, 2):
        picks = (part[:, None] == table_index).astype(own_rows.dtype)
        picked = jnp.dot(picks, own_rows, preferred_element_type=jnp.float32).astype(own_rows.dtype)
        own_parts.append(picked)
        previous_parts.append(shifted(picked, "ver", 1))
    own_slab = jnp.concatenate(own_parts)
    previous_slab = jnp.concatenate(previous_parts)
    partial_gram = lax.dot_general(
        own_slab, previous_slab, (((0,), (0,)), ((), ())), preferred_element_type=jnp.float32
    )
    cross_gram = summed_over(partial_gram, "z", core)
    frobenius = jnp.sqrt(jnp.sum(cross_gram * cross_gram) + 1e-06)
    iterate = cross_gram / frobenius
    iterate = lax.fori_loop(0, ROUGH_ITERS, newton_update(lax.Precision.HIGH), iterate)
    rotation = lax.fori_loop(ROUGH_ITERS, ITERS, newton_update(HIGHEST), iterate)
    identity_matrix = jnp.eye(width, dtype=jnp.float32)
    rotation = jnp.where(lax.axis_index("ver") == 0, identity_matrix, rotation)
    own_low = running_product(rotation, "ver", core).astype(jnp.bfloat16)
    prefix_low = joined_columns(own_low, swapped(own_low, "core", 1), core)
    return aligned_rows(embedding, prefix_low)


def solution(mesh):
    versions, rows = mesh.devices.shape
    cores = 2
    split_mesh = Mesh(mesh.devices.reshape(versions, rows // cores, cores), ("ver", "z", "core"))
    row = ("z", "core")
    return jax.shard_map(
        per_device,
        mesh=split_mesh,
        in_specs=(P("ver", row, None), P(row)),
        out_specs=P("ver", row, None),
        check_vma=False,
    )
```

```python
import jax
import jax.numpy as jnp
from jax import lax
from jax.experimental import pallas as pl
from jax.sharding import Mesh, PartitionSpec as P

ITERS = 12
ROUGH_ITERS = 10
HIGHEST = lax.Precision.HIGHEST


def shifted(value, axis, steps):
    count = lax.axis_size(axis)
    return lax.ppermute(value, axis, [(source, source + steps) for source in range(count - steps)])


def swapped(value, axis, mask):
    count = lax.axis_size(axis)
    return lax.ppermute(value, axis, [(source, source ^ mask) for source in range(count)])


def halves(matrix, core):
    half = matrix.shape[0] // 2
    return jnp.where(core == 0, matrix[:half], matrix[half:]), jnp.where(core == 0, matrix[half:], matrix[:half])


def joined(mine, other, core):
    return jnp.where(core == 0, jnp.concatenate([mine, other]), jnp.concatenate([other, mine]))


def summed_over(partial, axis, core):
    mine, other = halves(partial, core)
    mine = mine + swapped(other, "core", 1)
    count = lax.axis_size(axis)
    pieces = mine.reshape(count, mine.shape[0] // count, mine.shape[1])
    reduced = lax.all_to_all(pieces, axis, 0, 0, tiled=False).sum(0)
    copies = jnp.broadcast_to(reduced[None], (count,) + reduced.shape)
    mine = lax.all_to_all(copies, axis, 0, 0, tiled=False).reshape(mine.shape)
    return joined(mine, swapped(mine, "core", 1), core)


def newton_update(precision):
    def update(sweep_index, iterate):
        square = jnp.dot(iterate.T, iterate, precision=precision)
        return 1.5 * iterate - 0.5 * jnp.dot(iterate, square, precision=precision)

    return update


def column_half(matrix, core):
    half = matrix.shape[1] // 2
    return jnp.where(core == 0, matrix[:, :half], matrix[:, half:])


def joined_columns(mine, other, core):
    return jnp.where(
        core == 0, jnp.concatenate([mine, other], axis=1), jnp.concatenate([other, mine], axis=1)
    )


def running_product(rotation, axis, core):
    count, mine = (lax.axis_size(axis), lax.axis_index(axis))
    whole = rotation
    own_columns = column_half(rotation, core)
    steps = 1
    while steps < count:
        received = shifted(own_columns, axis, steps)
        longer = jnp.dot(whole, received, precision=HIGHEST)
        own_columns = jnp.where(mine >= steps, longer, own_columns)
        steps *= 2
        if steps < count:
            whole = joined_columns(own_columns, swapped(own_columns, "core", 1), core)
    return own_columns


def aligned_block(rows_ref, prefix_ref, out_ref):
    product = jnp.dot(rows_ref[...], prefix_ref[...], preferred_element_type=jnp.float32)
    out_ref[...] = product.astype(out_ref.dtype)


def aligned_rows(embedding, prefix_low):
    _, rows, width = embedding.shape
    block = 512
    return pl.pallas_call(
        aligned_block,
        grid=(rows // block,),
        in_specs=[
            pl.BlockSpec((None, block, width), lambda i: (0, i, 0)),
            pl.BlockSpec((width, width), lambda i: (0, 0)),
        ],
        out_specs=pl.BlockSpec((None, block, width), lambda i: (0, i, 0)),
        out_shape=jax.ShapeDtypeStruct(embedding.shape, embedding.dtype),
    )(embedding, prefix_low)


def per_device(embedding, anchor_rows):
    own_rows = embedding[0]
    width = own_rows.shape[1]
    core = lax.axis_index("core")
    row_index = lax.axis_index("z") * lax.axis_size("core") + core
    positions = anchor_rows - row_index * own_rows.shape[0]
    table_index = jnp.arange(own_rows.shape[0], dtype=positions.dtype)[None, :]
    own_parts, previous_parts = [], []
    for part in jnp.split(positions, 2):
        picks = (part[:, None] == table_index).astype(own_rows.dtype)
        picked = jnp.dot(picks, own_rows, preferred_element_type=jnp.float32).astype(own_rows.dtype)
        own_parts.append(picked)
        previous_parts.append(shifted(picked, "ver", 1))
    own_slab = jnp.concatenate(own_parts)
    previous_slab = jnp.concatenate(previous_parts)
    partial_gram = lax.dot_general(
        own_slab, previous_slab, (((0,), (0,)), ((), ())), preferred_element_type=jnp.float32
    )
    cross_gram = summed_over(partial_gram, "z", core)
    frobenius = jnp.sqrt(jnp.sum(cross_gram * cross_gram) + 1e-06)
    iterate = cross_gram / frobenius
    iterate = lax.fori_loop(0, ROUGH_ITERS, newton_update(lax.Precision.HIGH), iterate)
    for sweep_index in range(ROUGH_ITERS, ITERS):
        iterate = newton_update(HIGHEST)(sweep_index, iterate)
    rotation = iterate
    identity_matrix = jnp.eye(width, dtype=jnp.float32)
    rotation = jnp.where(lax.axis_index("ver") == 0, identity_matrix, rotation)
    own_low = running_product(rotation, "ver", core).astype(jnp.bfloat16)
    prefix_low = joined_columns(own_low, swapped(own_low, "core", 1), core)
    return aligned_rows(embedding, prefix_low)


def solution(mesh):
    versions, rows = mesh.devices.shape
    cores = 2
    split_mesh = Mesh(mesh.devices.reshape(versions, rows // cores, cores), ("ver", "z", "core"))
    row = ("z", "core")
    return jax.shard_map(
        per_device,
        mesh=split_mesh,
        in_specs=(P("ver", row, None), P(row)),
        out_specs=P("ver", row, None),
        check_vma=False,
    )
```

```python
import jax
import jax.numpy as jnp
from jax import lax
from jax.experimental import pallas as pl
from jax.sharding import Mesh, PartitionSpec as P

ITERS = 12
ROUGH_ITERS = 10
HIGHEST = lax.Precision.HIGHEST


def shifted(value, axis, steps):
    count = lax.axis_size(axis)
    return lax.ppermute(value, axis, [(source, source + steps) for source in range(count - steps)])


def swapped(value, axis, mask):
    count = lax.axis_size(axis)
    return lax.ppermute(value, axis, [(source, source ^ mask) for source in range(count)])


def halves(matrix, core):
    half = matrix.shape[0] // 2
    return jnp.where(core == 0, matrix[:half], matrix[half:]), jnp.where(core == 0, matrix[half:], matrix[:half])


def joined(mine, other, core):
    return jnp.where(core == 0, jnp.concatenate([mine, other]), jnp.concatenate([other, mine]))


def summed_over(partial, axis, core):
    mine, other = halves(partial, core)
    mine = mine + swapped(other, "core", 1)
    count = lax.axis_size(axis)
    pieces = mine.reshape(count, mine.shape[0] // count, mine.shape[1])
    reduced = lax.all_to_all(pieces, axis, 0, 0, tiled=False).sum(0)
    copies = jnp.broadcast_to(reduced[None], (count,) + reduced.shape)
    mine = lax.all_to_all(copies, axis, 0, 0, tiled=False).reshape(mine.shape)
    return joined(mine, swapped(mine, "core", 1), core)


def newton_update(precision):
    def update(sweep_index, iterate):
        square = jnp.dot(iterate.T, iterate, precision=precision)
        return 1.5 * iterate - 0.5 * jnp.dot(iterate, square, precision=precision)

    return update


def column_half(matrix, core):
    half = matrix.shape[1] // 2
    return jnp.where(core == 0, matrix[:, :half], matrix[:, half:])


def joined_columns(mine, other, core):
    return jnp.where(
        core == 0, jnp.concatenate([mine, other], axis=1), jnp.concatenate([other, mine], axis=1)
    )


def running_product(rotation, axis, core):
    count, mine = (lax.axis_size(axis), lax.axis_index(axis))
    whole = rotation
    own_columns = column_half(rotation, core)
    steps = 1
    while steps < count:
        received = shifted(own_columns, axis, steps)
        longer = jnp.dot(whole, received, precision=HIGHEST)
        own_columns = jnp.where(mine >= steps, longer, own_columns)
        steps *= 2
        if steps < count:
            whole = joined_columns(own_columns, swapped(own_columns, "core", 1), core)
    return own_columns


def aligned_block(rows_ref, prefix_ref, out_ref):
    product = jnp.dot(rows_ref[...], prefix_ref[...], preferred_element_type=jnp.float32)
    out_ref[...] = product.astype(out_ref.dtype)


def aligned_rows(embedding, prefix_low):
    _, rows, width = embedding.shape
    block = 512
    return pl.pallas_call(
        aligned_block,
        grid=(rows // block,),
        in_specs=[
            pl.BlockSpec((None, block, width), lambda i: (0, i, 0)),
            pl.BlockSpec((width, width), lambda i: (0, 0)),
        ],
        out_specs=pl.BlockSpec((None, block, width), lambda i: (0, i, 0)),
        out_shape=jax.ShapeDtypeStruct(embedding.shape, embedding.dtype),
    )(embedding, prefix_low)


def per_device(embedding, anchor_rows):
    own_rows = embedding[0]
    width = own_rows.shape[1]
    core = lax.axis_index("core")
    row_index = lax.axis_index("z") * lax.axis_size("core") + core
    positions = anchor_rows - row_index * own_rows.shape[0]
    table_index = jnp.arange(own_rows.shape[0], dtype=positions.dtype)[None, :]
    own_parts, previous_parts = [], []
    for part in jnp.split(positions, 4):
        picks = (part[:, None] == table_index).astype(own_rows.dtype)
        picked = jnp.dot(picks, own_rows, preferred_element_type=jnp.float32).astype(own_rows.dtype)
        own_parts.append(picked)
        previous_parts.append(shifted(picked, "ver", 1))
    own_slab = jnp.concatenate(own_parts)
    previous_slab = jnp.concatenate(previous_parts)
    partial_gram = lax.dot_general(
        own_slab, previous_slab, (((0,), (0,)), ((), ())), preferred_element_type=jnp.float32
    )
    cross_gram = summed_over(partial_gram, "z", core)
    frobenius = jnp.sqrt(jnp.sum(cross_gram * cross_gram) + 1e-06)
    iterate = cross_gram / frobenius
    iterate = lax.fori_loop(0, ROUGH_ITERS, newton_update(lax.Precision.HIGH), iterate)
    for sweep_index in range(ROUGH_ITERS, ITERS):
        iterate = newton_update(HIGHEST)(sweep_index, iterate)
    rotation = iterate
    identity_matrix = jnp.eye(width, dtype=jnp.float32)
    rotation = jnp.where(lax.axis_index("ver") == 0, identity_matrix, rotation)
    own_low = running_product(rotation, "ver", core).astype(jnp.bfloat16)
    prefix_low = joined_columns(own_low, swapped(own_low, "core", 1), core)
    return aligned_rows(embedding, prefix_low)


def solution(mesh):
    versions, rows = mesh.devices.shape
    cores = 2
    split_mesh = Mesh(mesh.devices.reshape(versions, rows // cores, cores), ("ver", "z", "core"))
    row = ("z", "core")
    return jax.shard_map(
        per_device,
        mesh=split_mesh,
        in_specs=(P("ver", row, None), P(row)),
        out_specs=P("ver", row, None),
        check_vma=False,
    )
```
